256 devices in a mesh: seq: 8 (over z_lo, x), chan: 32 (over y, z_hi, core).
Axes of the slice: x: 4, y: 4, z: 8 (z_hi: 4, z_lo: 2; z = z_hi * 2 + z_lo), core: 2. Of those that a mesh axis runs over, the one named last changes fastest.
Arguments:
- tokens: bfloat16 [8192, 4096], P('seq', 'chan'), may hold values from -6 to 6
- in_weight: bfloat16 [4096, 3, 4096], P(None, None, 'chan'), may hold values from -0.09375 to 0.09375
- short_taps: float32 [3, 3, 4096], P(None, None, 'chan'), may hold values from -3 to 3
- filter_taps: float32 [8192, 4096], P('seq', 'chan'), may hold values from -1 to 1
- skip_gain: float32 [4096], P('chan'), may hold values from -4 to 4
- out_weight: bfloat16 [4096, 4096], P('chan'), may hold values from -0.1875 to 0.1875
Outputs:
- layer_out: bfloat16 [8192, 4096], P('seq', 'chan')
The draws below stay inside these ranges and needn't reach their ends.
All inputs are finite; a program needn't handle non-finite values.
Results may differ from the reference program's by a relative error of at most 0.007.
Values may be sent and summed in bfloat16 or wider, within the bound.
No kernel may reach another device: no remote copies, remote signals or barrier semaphores. Data moves between devices by JAX's collectives and lax.ppermute only.
A program may use at most 128 MiB of HBM per device.

```python
import math
import jax
import jax.numpy as jnp

EMBED_DIMENSION = 4096
STEP_COUNT = 8192


def draw_filter_taps(key, part):
    derived_prng_streams = jax.random.split(key, 6)
    element_ordinal = jnp.arange(STEP_COUNT, dtype=jnp.float32)[:, None]
    quick_share = 0.5
    quick_mask = jax.random.uniform(derived_prng_streams[0], (1, EMBED_DIMENSION)) < quick_share
    quick_span = jax.random.uniform(derived_prng_streams[1], (1, EMBED_DIMENSION), minval=30.0, maxval=50.0)
    slow_span = STEP_COUNT * jnp.exp(jax.random.uniform(derived_prng_streams[2], (1, EMBED_DIMENSION), minval=math.log(2.0), maxval=math.log(6.0)))
    decay_span = jnp.where(quick_mask, quick_span, slow_span)
    impulse_start = jax.random.randint(derived_prng_streams[3], (3, EMBED_DIMENSION), 0, STEP_COUNT).astype(jnp.float32)
    impulse_keep_mask = jax.random.uniform(derived_prng_streams[4], (3, EMBED_DIMENSION), minval=0.6, maxval=0.8)
    scaling_coefficient = jnp.ones((STEP_COUNT, EMBED_DIMENSION), jnp.float32)
    for impulse_signal in range(3):
        scaling_coefficient = scaling_coefficient * jnp.where(element_ordinal >= impulse_start[impulse_signal][None, :], impulse_keep_mask[impulse_signal][None, :], 1.0)
    envelope = jnp.exp(-element_ordinal / decay_span) * scaling_coefficient / jnp.sqrt(jnp.minimum(decay_span, float(STEP_COUNT)))
    rough_part = jnp.clip(jax.random.normal(derived_prng_streams[5], (STEP_COUNT, EMBED_DIMENSION)), -4.0, 4.0)
    return (envelope * rough_part).astype(jnp.float32)


def raised(drawn, stream_key, source, target, blocks, factor):
    def block_of(dim):
        return (jnp.arange(drawn.shape[dim]) // (drawn.shape[dim] // blocks)).reshape((-1,) + (1,) * (drawn.ndim - 1 - dim))

    first = jax.random.permutation(stream_key, blocks)[block_of(target)]
    other_side = (block_of(target) + blocks // 2) % blocks
    return jnp.where((block_of(source) == first) | (block_of(source) == other_side), factor * drawn, drawn)


def block_levels(stream_key, extent, cuts, low, high):
    def one(axis_at, shards_of):
        steps = jax.random.uniform(jax.random.fold_in(jax.random.fold_in(stream_key, 6), axis_at), (shards_of,), jnp.float32, low / len(cuts), high / len(cuts))
        return jnp.repeat(jnp.exp(steps), extent[axis_at] // shards_of).reshape((-1,) + (1,) * (len(extent) - axis_at - 1))

    gain = one(*cuts[0])
    for cut in cuts[1:]:
        gain = gain * one(*cut)
    return gain


def centred(key, shape, deviation, most, cuts=(), kind=jnp.bfloat16):
    array = deviation * jax.random.normal(key, shape, jnp.float32)
    if cuts:
        array = array * block_levels(key, shape, cuts, -0.22, 0.18)
    return jnp.clip(array, -most, most).astype(kind)


def bell_draw_with(own_key, shape, deviation, reach, cuts, heavy, kind=jnp.bfloat16):
    array = deviation * jax.random.normal(own_key, shape, jnp.float32)
    if cuts:
        array = array * block_levels(own_key, shape, cuts, -0.22, 0.18)
    return jnp.clip(raised(array, jax.random.fold_in(own_key, 3), *heavy), -reach, reach).astype(kind)


def setup_inputs(seed: int = 0) -> dict:
    seeds = jax.random.split(jax.random.key(seed), 7)
    tokens = centred(seeds[0], (STEP_COUNT, EMBED_DIMENSION), 1.0, 6.0, ((0, 8), (1, 32)))
    in_weight = centred(seeds[1], (EMBED_DIMENSION, 3, EMBED_DIMENSION), EMBED_DIMENSION ** -0.5, 0.09375, ((2, 32),))
    short_taps = centred(seeds[2], (3, 3, EMBED_DIMENSION), 0.6, 3.0, ((2, 32),), jnp.float32)
    filter_taps = draw_filter_taps(jax.random.fold_in(seeds[6], 71), 0)
    skip_gain = centred(seeds[4], (EMBED_DIMENSION,), 1.0, 4.0, ((0, 32),), jnp.float32)
    out_weight = bell_draw_with(seeds[5], (EMBED_DIMENSION, EMBED_DIMENSION), EMBED_DIMENSION ** -0.5, 0.1875, ((0, 32),), (0, 1, 32, 2.75))
    return {"tokens": tokens, "in_weight": in_weight, "short_taps": short_taps, "filter_taps": filter_taps, "skip_gain": skip_gain, "out_weight": out_weight}


def reference(tokens, in_weight, short_taps, filter_taps, skip_gain, out_weight):
    projected = jnp.dot(tokens, in_weight.reshape(EMBED_DIMENSION, 3 * EMBED_DIMENSION), preferred_element_type=jnp.float32)
    projected = projected.astype(jnp.bfloat16).reshape(STEP_COUNT, 3, EMBED_DIMENSION).astype(jnp.float32)
    padded = jnp.pad(projected, ((2, 0), (0, 0), (0, 0)))
    mixed = short_taps[0] * padded[2:] + short_taps[1] * padded[1:-1] + short_taps[2] * padded[:-2]
    gate_out = mixed[:, 0]
    signal = mixed[:, 1] * mixed[:, 2]
    block_width = max(EMBED_DIMENSION // 8, 1)
    pieces = []
    for block_start in range(0, EMBED_DIMENSION, block_width):
        signal_block = signal[:, block_start:block_start + block_width]
        filter_block = filter_taps[:, block_start:block_start + block_width]
        spectrum = jnp.fft.rfft(signal_block, n=2 * STEP_COUNT, axis=0) * jnp.fft.rfft(filter_block, n=2 * STEP_COUNT, axis=0)
        pieces.append(jnp.fft.irfft(spectrum, n=2 * STEP_COUNT, axis=0)[:STEP_COUNT])
    convolved = jnp.concatenate(pieces, axis=1)
    hidden = (gate_out * (convolved + skip_gain * signal)).astype(jnp.bfloat16)
    return jnp.dot(hidden, out_weight, preferred_element_type=jnp.float32).astype(jnp.bfloat16)
```

```python
import math

import jax
import jax.numpy as jnp
from jax import lax
from jax.sharding import PartitionSpec as P

COLS = 256


highest = lax.Precision.HIGHEST


def from_behind(shard, axis, by):
    size = lax.axis_size(axis)
    pairs = [(i, i + by) for i in range(size) if 0 <= i + by < size]
    return lax.ppermute(shard, axis, pairs)


def phase_table(row_count, col_count, period):
    row_index = jnp.arange(row_count, dtype=jnp.int32)[:, None]
    col_index = jnp.arange(col_count, dtype=jnp.int32)[None, :]
    angle = (row_index * col_index % period).astype(jnp.float32) * (2.0 * math.pi / period)
    return (jnp.cos(angle), jnp.sin(angle))


def real_transform(signal, cosine, sines, pattern):
    real_part = jnp.einsum(pattern, cosine, signal, precision=highest)
    imag_part = -jnp.einsum(pattern, sines, signal, precision=highest)
    return (real_part, imag_part)


def complex_transform(real_part, imag_part, cosine, sines, direction, pattern):
    cos_real = jnp.einsum(pattern, cosine, real_part, precision=highest)
    cos_imag = jnp.einsum(pattern, cosine, imag_part, precision=highest)
    sin_real = jnp.einsum(pattern, sines, real_part, precision=highest)
    sin_imag = jnp.einsum(pattern, sines, imag_part, precision=highest)
    return (cos_real - direction * sin_imag, cos_imag + direction * sin_real)


def rotate(real_part, imag_part, cosine, sines, direction):
    return (
        real_part * cosine - direction * imag_part * sines,
        imag_part * cosine + direction * real_part * sines,
    )


def spectrum_product(left, right):
    prod_real = left[0] * right[0] - left[1] * right[1]
    prod_imag = left[0] * right[1] + left[1] * right[0]
    return (prod_real, prod_imag)


def real_inverse(real_part, imag_part, cosine, sines, pattern, length):
    return (
        jnp.einsum(pattern, cosine, real_part, precision=highest)
        - jnp.einsum(pattern, sines, imag_part, precision=highest)
    ) / length


def tables(length):
    full_rows = 2 * length // COLS
    half_rows = full_rows // 2
    period = 2 * length
    first = phase_table(full_rows, half_rows, full_rows)
    twist_cos, twist_sin = phase_table(full_rows, COLS, period)
    twist = (twist_cos[:, :, None], twist_sin[:, :, None])
    second = phase_table(COLS, COLS, COLS)
    last = phase_table(half_rows, full_rows, full_rows)
    return first, twist, second, last


def forward_spectrum(whole_seq, first, twist, second):
    length, narrow = whole_seq.shape
    half_rows = 2 * length // COLS // 2
    laid_out = whole_seq.reshape(half_rows, COLS, narrow)
    real_part, imag_part = real_transform(laid_out, first[0], first[1], "kn,nmc->kmc")
    real_part, imag_part = rotate(real_part, imag_part, twist[0], twist[1], -1.0)
    return complex_transform(
        real_part, imag_part, second[0], second[1], -1.0, "kn,anc->akc"
    )


def inverse_spectrum(real_part, imag_part, twist, second, last, length, narrow):
    real_part, imag_part = complex_transform(
        real_part, imag_part, second[0], second[1], 1.0, "kn,anc->akc"
    )
    real_part, imag_part = rotate(real_part, imag_part, twist[0], twist[1], 1.0)
    values = real_inverse(real_part, imag_part, last[0], last[1], "nk,kmc->nmc", 2 * length)
    return values.reshape(length, narrow)


def to_whole_seq(shard):
    return lax.all_to_all(shard, "seq", split_axis=1, concat_axis=0, tiled=True)


def body(tokens, in_weight, short_taps, filter_taps, skip_gain, out_weight):
    tok_count = tokens.shape[0]
    chan_count = in_weight.shape[2]
    out_block = lax.all_to_all(out_weight, "chan", split_axis=1, concat_axis=0, tiled=True)
    whole_filter = to_whole_seq(filter_taps)
    length, narrow = whole_filter.shape
    first, twist, second, last = tables(length)
    filter_spec = forward_spectrum(whole_filter, first, twist, second)
    flat_weight = in_weight.reshape(in_weight.shape[0], 3 * chan_count)
    projected = jnp.dot(
        lax.all_gather(tokens, "chan", axis=1, tiled=True),
        flat_weight,
        preferred_element_type=jnp.float32,
    )
    projected = projected.astype(jnp.bfloat16).reshape(tok_count, 3, chan_count)
    previous = from_behind(projected[-2:], "seq", 1)
    extended = jnp.concatenate([previous, projected], axis=0).astype(jnp.float32)
    short_mixed = (
        short_taps[0] * extended[2:]
        + short_taps[1] * extended[1:-1]
        + short_taps[2] * extended[:-2]
    )
    gate_out = short_mixed[:, 0]
    signal = short_mixed[:, 1] * short_mixed[:, 2]
    signal_spec = forward_spectrum(to_whole_seq(signal), first, twist, second)
    real_part, imag_part = spectrum_product(signal_spec, filter_spec)
    values = inverse_spectrum(real_part, imag_part, twist, second, last, length, narrow)
    convolved = lax.all_to_all(values, "seq", split_axis=0, concat_axis=1, tiled=True)
    hidden = (gate_out * (convolved + skip_gain * signal)).astype(jnp.bfloat16)
    full_hidden = lax.all_gather(hidden, "chan", axis=1, tiled=True)
    layer_out = jnp.dot(full_hidden, out_block, preferred_element_type=jnp.float32)
    return layer_out.astype(jnp.bfloat16)


def solution(mesh):
    in_specs = (
        P("seq", "chan"),
        P(None, None, "chan"),
        P(None, None, "chan"),
        P("seq", "chan"),
        P("chan"),
        P("chan", None),
    )
    out_specs = P("seq", "chan")
    return jax.shard_map(body, mesh=mesh, in_specs=in_specs, out_specs=out_specs, check_vma=False)
```

```python
import math

import jax
import jax.numpy as jnp
from jax import lax
from jax.sharding import PartitionSpec as P

COLS = 256


highest = lax.Precision.HIGHEST


def from_behind(shard, axis, by):
    size = lax.axis_size(axis)
    pairs = [(i, i + by) for i in range(size) if 0 <= i + by < size]
    return lax.ppermute(shard, axis, pairs)


def phase_table(row_count, col_count, period):
    row_index = jnp.arange(row_count, dtype=jnp.int32)[:, None]
    col_index = jnp.arange(col_count, dtype=jnp.int32)[None, :]
    angle = (row_index * col_index % period).astype(jnp.float32) * (2.0 * math.pi / period)
    return (jnp.cos(angle), jnp.sin(angle))


def real_transform(signal, cosine, sines, pattern):
    real_part = jnp.einsum(pattern, cosine, signal, precision=highest)
    imag_part = -jnp.einsum(pattern, sines, signal, precision=highest)
    return (real_part, imag_part)


def complex_transform(real_part, imag_part, cosine, sines, direction, pattern):
    cos_real = jnp.einsum(pattern, cosine, real_part, precision=highest)
    cos_imag = jnp.einsum(pattern, cosine, imag_part, precision=highest)
    sin_real = jnp.einsum(pattern, sines, real_part, precision=highest)
    sin_imag = jnp.einsum(pattern, sines, imag_part, precision=highest)
    return (cos_real - direction * sin_imag, cos_imag + direction * sin_real)


def rotate(real_part, imag_part, cosine, sines, direction):
    return (
        real_part * cosine - direction * imag_part * sines,
        imag_part * cosine + direction * real_part * sines,
    )


def spectrum_product(left, right):
    prod_real = left[0] * right[0] - left[1] * right[1]
    prod_imag = left[0] * right[1] + left[1] * right[0]
    return (prod_real, prod_imag)


def real_inverse(real_part, imag_part, cosine, sines, pattern, length):
    return (
        jnp.einsum(pattern, cosine, real_part, precision=highest)
        - jnp.einsum(pattern, sines, imag_part, precision=highest)
    ) / length


def tables(length):
    full_rows = 2 * length // COLS
    half_rows = full_rows // 2
    period = 2 * length
    first = phase_table(full_rows, half_rows, full_rows)
    twist_cos, twist_sin = phase_table(full_rows, COLS, period)
    twist = (twist_cos[:, :, None], twist_sin[:, :, None])
    second = phase_table(COLS, COLS, COLS)
    last = phase_table(half_rows, full_rows, full_rows)
    return first, twist, second, last


def forward_spectrum(whole_seq, first, twist, second):
    length, narrow = whole_seq.shape
    half_rows = 2 * length // COLS // 2
    laid_out = whole_seq.reshape(half_rows, COLS, narrow)
    real_part, imag_part = real_transform(laid_out, first[0], first[1], "kn,nmc->kmc")
    real_part, imag_part = rotate(real_part, imag_part, twist[0], twist[1], -1.0)
    return complex_transform(
        real_part, imag_part, second[0], second[1], -1.0, "kn,anc->akc"
    )


def inverse_spectrum(real_part, imag_part, twist, second, last, length, narrow):
    real_part, imag_part = complex_transform(
        real_part, imag_part, second[0], second[1], 1.0, "kn,anc->akc"
    )
    real_part, imag_part = rotate(real_part, imag_part, twist[0], twist[1], 1.0)
    values = real_inverse(real_part, imag_part, last[0], last[1], "nk,kmc->nmc", 2 * length)
    return values.reshape(length, narrow)


def to_whole_seq(shard):
    return lax.all_to_all(shard, "seq", split_axis=1, concat_axis=0, tiled=True)


def layer(tokens, in_weight, short_taps, filter_taps, skip_gain, out_weight):
    tok_count = tokens.shape[0]
    chan_count = in_weight.shape[2]
    whole_tokens = lax.all_gather(tokens, "chan", axis=1, tiled=True)
    out_block = lax.all_to_all(out_weight, "chan", split_axis=1, concat_axis=0, tiled=True)
    whole_filter = to_whole_seq(filter_taps)
    length, narrow = whole_filter.shape
    first, twist, second, last = tables(length)
    filter_tables = lax.optimization_barrier((first, twist, second))
    filter_spec = forward_spectrum(whole_filter, *filter_tables)
    flat_weight = in_weight.reshape(in_weight.shape[0], 3 * chan_count)
    projected = jnp.dot(whole_tokens, flat_weight, preferred_element_type=jnp.float32)
    projected = projected.astype(jnp.bfloat16).reshape(tok_count, 3, chan_count)
    previous = from_behind(projected[-2:], "seq", 1)
    extended = jnp.concatenate([previous, projected], axis=0).astype(jnp.float32)
    short_mixed = (
        short_taps[0] * extended[2:]
        + short_taps[1] * extended[1:-1]
        + short_taps[2] * extended[:-2]
    )
    gate_out = short_mixed[:, 0]
    signal = short_mixed[:, 1] * short_mixed[:, 2]
    signal_spec = forward_spectrum(to_whole_seq(signal), first, twist, second)
    real_part, imag_part = spectrum_product(signal_spec, filter_spec)
    values = inverse_spectrum(real_part, imag_part, twist, second, last, length, narrow)
    convolved = lax.all_to_all(values, "seq", split_axis=0, concat_axis=1, tiled=True)
    hidden = (gate_out * (convolved + skip_gain * signal)).astype(jnp.bfloat16)
    full_hidden = lax.all_gather(hidden, "chan", axis=1, tiled=True)
    layer_out = jnp.dot(full_hidden, out_block, preferred_element_type=jnp.float32)
    return layer_out.astype(jnp.bfloat16)


def solution(mesh):
    in_specs = (
        P("seq", "chan"),
        P(None, None, "chan"),
        P(None, None, "chan"),
        P("seq", "chan"),
        P("chan"),
        P("chan", None),
    )
    out_specs = P("seq", "chan")
    return jax.shard_map(layer, mesh=mesh, in_specs=in_specs, out_specs=out_specs, check_vma=False)
```

```python
import math

import jax
import jax.numpy as jnp
from jax import lax
from jax.sharding import PartitionSpec as P

COLS = 256


highest = lax.Precision.HIGH


def from_behind(shard, axis, by):
    size = lax.axis_size(axis)
    pairs = [(i, i + by) for i in range(size) if 0 <= i + by < size]
    return lax.ppermute(shard, axis, pairs)


def phase_table(row_count, col_count, period):
    row_index = jnp.arange(row_count, dtype=jnp.int32)[:, None]
    col_index = jnp.arange(col_count, dtype=jnp.int32)[None, :]
    angle = (row_index * col_index % period).astype(jnp.float32) * (2.0 * math.pi / period)
    return (jnp.cos(angle), jnp.sin(angle))


def real_transform(signal, cosine, sines, pattern):
    real_part = jnp.einsum(pattern, cosine, signal, precision=highest)
    imag_part = -jnp.einsum(pattern, sines, signal, precision=highest)
    return (real_part, imag_part)


def complex_transform(real_part, imag_part, cosine, sines, direction, pattern):
    cos_real = jnp.einsum(pattern, cosine, real_part, precision=highest)
    cos_imag = jnp.einsum(pattern, cosine, imag_part, precision=highest)
    sin_real = jnp.einsum(pattern, sines, real_part, precision=highest)
    sin_imag = jnp.einsum(pattern, sines, imag_part, precision=highest)
    return (cos_real - direction * sin_imag, cos_imag + direction * sin_real)


def rotate(real_part, imag_part, cosine, sines, direction):
    return (
        real_part * cosine - direction * imag_part * sines,
        imag_part * cosine + direction * real_part * sines,
    )


def spectrum_product(left, right):
    prod_real = left[0] * right[0] - left[1] * right[1]
    prod_imag = left[0] * right[1] + left[1] * right[0]
    return (prod_real, prod_imag)


def real_inverse(real_part, imag_part, cosine, sines, pattern, length):
    return (
        jnp.einsum(pattern, cosine, real_part, precision=highest)
        - jnp.einsum(pattern, sines, imag_part, precision=highest)
    ) / length


def tables(length):
    full_rows = 2 * length // COLS
    half_rows = full_rows // 2
    period = 2 * length
    first = phase_table(full_rows, half_rows, full_rows)
    twist_cos, twist_sin = phase_table(full_rows, COLS, period)
    twist = (twist_cos[:, :, None], twist_sin[:, :, None])
    second = phase_table(COLS, COLS, COLS)
    last = phase_table(half_rows, full_rows, full_rows)
    return first, twist, second, last


def forward_spectrum(whole_seq, first, twist, second):
    length, narrow = whole_seq.shape
    half_rows = 2 * length // COLS // 2
    laid_out = whole_seq.reshape(half_rows, COLS, narrow)
    real_part, imag_part = real_transform(laid_out, first[0], first[1], "kn,nmc->kmc")
    real_part, imag_part = rotate(real_part, imag_part, twist[0], twist[1], -1.0)
    return complex_transform(
        real_part, imag_part, second[0], second[1], -1.0, "kn,anc->akc"
    )


def inverse_spectrum(real_part, imag_part, twist, second, last, length, narrow):
    real_part, imag_part = complex_transform(
        real_part, imag_part, second[0], second[1], 1.0, "kn,anc->akc"
    )
    real_part, imag_part = rotate(real_part, imag_part, twist[0], twist[1], 1.0)
    values = real_inverse(real_part, imag_part, last[0], last[1], "nk,kmc->nmc", 2 * length)
    return values.reshape(length, narrow)


def to_whole_seq(shard):
    return lax.all_to_all(shard, "seq", split_axis=1, concat_axis=0, tiled=True)


def layer(tokens, in_weight, short_taps, filter_taps, skip_gain, out_weight):
    tok_count = tokens.shape[0]
    chan_count = in_weight.shape[2]
    whole_tokens = lax.all_gather(tokens, "chan", axis=1, tiled=True)
    out_block = lax.all_to_all(out_weight, "chan", split_axis=1, concat_axis=0, tiled=True)
    whole_filter = to_whole_seq(filter_taps)
    length, narrow = whole_filter.shape
    first, twist, second, last = tables(length)
    filter_tables = lax.optimization_barrier((first, twist, second))
    filter_spec = forward_spectrum(whole_filter, *filter_tables)
    flat_weight = in_weight.reshape(in_weight.shape[0], 3 * chan_count)
    projected = jnp.dot(whole_tokens, flat_weight, preferred_element_type=jnp.float32)
    projected = projected.astype(jnp.bfloat16).reshape(tok_count, 3, chan_count)
    previous = from_behind(projected[-2:], "seq", 1)
    extended = jnp.concatenate([previous, projected], axis=0).astype(jnp.float32)
    short_mixed = (
        short_taps[0] * extended[2:]
        + short_taps[1] * extended[1:-1]
        + short_taps[2] * extended[:-2]
    )
    gate_out = short_mixed[:, 0]
    signal = short_mixed[:, 1] * short_mixed[:, 2]
    whole_signal = to_whole_seq(signal)
    signal_spec = forward_spectrum(whole_signal, first, twist, second)
    real_part, imag_part = spectrum_product(signal_spec, filter_spec)
    values = inverse_spectrum(real_part, imag_part, twist, second, last, length, narrow)
    convolved = lax.all_to_all(values, "seq", split_axis=0, concat_axis=1, tiled=True)
    hidden = (gate_out * (convolved + skip_gain * signal)).astype(jnp.bfloat16)
    full_hidden = lax.all_gather(hidden, "chan", axis=1, tiled=True)
    layer_out = jnp.dot(full_hidden, out_block, preferred_element_type=jnp.float32)
    return layer_out.astype(jnp.bfloat16)


def solution(mesh):
    in_specs = (
        P("seq", "chan"),
        P(None, None, "chan"),
        P(None, None, "chan"),
        P("seq", "chan"),
        P("chan"),
        P("chan", None),
    )
    out_specs = P("seq", "chan")
    return jax.shard_map(layer, mesh=mesh, in_specs=in_specs, out_specs=out_specs, check_vma=False)
```

```python
import math

import jax
import jax.numpy as jnp
from jax import lax
from jax.sharding import PartitionSpec as P

COLS = 256


highest = lax.Precision.HIGH


def from_behind(shard, axis, by):
    size = lax.axis_size(axis)
    pairs = [(i, i + by) for i in range(size) if 0 <= i + by < size]
    return lax.ppermute(shard, axis, pairs)


def phase_table(row_count, col_count, period):
    row_index = jnp.arange(row_count, dtype=jnp.int32)[:, None]
    col_index = jnp.arange(col_count, dtype=jnp.int32)[None, :]
    angle = (row_index * col_index % period).astype(jnp.float32) * (2.0 * math.pi / period)
    return (jnp.cos(angle), jnp.sin(angle))


def real_transform(signal, cosine, sines, pattern):
    real_part = jnp.einsum(pattern, cosine, signal, precision=highest)
    imag_part = -jnp.einsum(pattern, sines, signal, precision=highest)
    return (real_part, imag_part)


def complex_transform(real_part, imag_part, cosine, sines, direction, pattern):
    cos_real = jnp.einsum(pattern, cosine, real_part, precision=highest)
    cos_imag = jnp.einsum(pattern, cosine, imag_part, precision=highest)
    sin_real = jnp.einsum(pattern, sines, real_part, precision=highest)
    sin_imag = jnp.einsum(pattern, sines, imag_part, precision=highest)
    return (cos_real - direction * sin_imag, cos_imag + direction * sin_real)


def rotate(real_part, imag_part, cosine, sines, direction):
    return (
        real_part * cosine - direction * imag_part * sines,
        imag_part * cosine + direction * real_part * sines,
    )


def spectrum_product(left, right):
    prod_real = left[0] * right[0] - left[1] * right[1]
    prod_imag = left[0] * right[1] + left[1] * right[0]
    return (prod_real, prod_imag)


def real_inverse(real_part, imag_part, cosine, sines, pattern, length):
    return (
        jnp.einsum(pattern, cosine, real_part, precision=highest)
        - jnp.einsum(pattern, sines, imag_part, precision=highest)
    ) / length


def tables(length):
    full_rows = 2 * length // COLS
    half_rows = full_rows // 2
    period = 2 * length
    first = phase_table(full_rows, half_rows, full_rows)
    twist_cos, twist_sin = phase_table(full_rows, COLS, period)
    twist = (twist_cos[:, :, None], twist_sin[:, :, None])
    second = phase_table(COLS, COLS, COLS)
    last = phase_table(half_rows, full_rows, full_rows)
    return first, twist, second, last


def forward_spectrum(whole_seq, first, twist, second):
    length, narrow = whole_seq.shape
    half_rows = 2 * length // COLS // 2
    laid_out = whole_seq.reshape(half_rows, COLS, narrow)
    real_part, imag_part = real_transform(laid_out, first[0], first[1], "kn,nmc->kmc")
    real_part, imag_part = rotate(real_part, imag_part, twist[0], twist[1], -1.0)
    return complex_transform(
        real_part, imag_part, second[0], second[1], -1.0, "kn,anc->akc"
    )


def inverse_spectrum(real_part, imag_part, twist, second, last, length, narrow):
    real_part, imag_part = complex_transform(
        real_part, imag_part, second[0], second[1], 1.0, "kn,anc->akc"
    )
    real_part, imag_part = rotate(real_part, imag_part, twist[0], twist[1], 1.0)
    values = real_inverse(real_part, imag_part, last[0], last[1], "nk,kmc->nmc", 2 * length)
    return values.reshape(length, narrow)


def project(rows, weight):
    groups, chan_count = weight.shape[1], weight.shape[2]
    flat_weight = weight.reshape(weight.shape[0], groups * chan_count)
    out = jnp.dot(rows, flat_weight, preferred_element_type=jnp.float32)
    return out.astype(jnp.bfloat16).reshape(rows.shape[0], groups, chan_count)


def short_conv(own, behind, taps):
    extended = jnp.concatenate([behind, own], axis=0).astype(jnp.float32)
    return taps[0] * extended[2:] + taps[1] * extended[1:-1] + taps[2] * extended[:-2]


def to_whole_seq(shard):
    return lax.all_to_all(shard, "seq", split_axis=1, concat_axis=0, tiled=True)


def layer(tokens, in_weight, short_taps, filter_taps, skip_gain, out_weight):
    whole_tokens = lax.all_gather(tokens, "chan", axis=1, tiled=True)
    out_block = lax.all_to_all(out_weight, "chan", split_axis=1, concat_axis=0, tiled=True)
    whole_filter = to_whole_seq(filter_taps)
    length, narrow = whole_filter.shape
    first, twist, second, last = tables(length)
    filter_tables = lax.optimization_barrier((first, twist, second))
    filter_spec = forward_spectrum(whole_filter, *filter_tables)
    tail = project(whole_tokens[-2:], in_weight)
    previous = from_behind(tail, "seq", 1)
    value_groups = project(whole_tokens, in_weight[:, 1:])
    mixed_values = short_conv(value_groups, previous[:, 1:], short_taps[:, 1:])
    signal = mixed_values[:, 0] * mixed_values[:, 1]
    whole_signal = to_whole_seq(signal)
    gate_group = project(whole_tokens, in_weight[:, :1])
    gate_out = short_conv(gate_group, previous[:, :1], short_taps[:, :1])[:, 0]
    signal_spec = forward_spectrum(whole_signal, first, twist, second)
    real_part, imag_part = spectrum_product(signal_spec, filter_spec)
    values = inverse_spectrum(real_part, imag_part, twist, second, last, length, narrow)
    convolved = lax.all_to_all(values, "seq", split_axis=0, concat_axis=1, tiled=True)
    hidden = (gate_out * (convolved + skip_gain * signal)).astype(jnp.bfloat16)
    full_hidden = lax.all_gather(hidden, "chan", axis=1, tiled=True)
    layer_out = jnp.dot(full_hidden, out_block, preferred_element_type=jnp.float32)
    return layer_out.astype(jnp.bfloat16)


def solution(mesh):
    in_specs = (
        P("seq", "chan"),
        P(None, None, "chan"),
        P(None, None, "chan"),
        P("seq", "chan"),
        P("chan"),
        P("chan", None),
    )
    out_specs = P("seq", "chan")
    return jax.shard_map(layer, mesh=mesh, in_specs=in_specs, out_specs=out_specs, check_vma=False)
```

```python
import math

import jax
import jax.numpy as jnp
from jax import lax
from jax.sharding import PartitionSpec as P

COLS = 256


highest = lax.Precision.HIGH


def from_behind(shard, axis, by):
    size = lax.axis_size(axis)
    pairs = [(i, i + by) for i in range(size) if 0 <= i + by < size]
    return lax.ppermute(shard, axis, pairs)


def phase_table(row_count, col_count, period):
    row_index = jnp.arange(row_count, dtype=jnp.int32)[:, None]
    col_index = jnp.arange(col_count, dtype=jnp.int32)[None, :]
    angle = (row_index * col_index % period).astype(jnp.float32) * (2.0 * math.pi / period)
    return (jnp.cos(angle), jnp.sin(angle))


def real_transform(signal, cosine, sines, pattern):
    real_part = jnp.einsum(pattern, cosine, signal, precision=highest)
    imag_part = -jnp.einsum(pattern, sines, signal, precision=highest)
    return (real_part, imag_part)


def complex_transform(real_part, imag_part, cosine, sines, direction, pattern):
    cos_real = jnp.einsum(pattern, cosine, real_part, precision=highest)
    cos_imag = jnp.einsum(pattern, cosine, imag_part, precision=highest)
    sin_real = jnp.einsum(pattern, sines, real_part, precision=highest)
    sin_imag = jnp.einsum(pattern, sines, imag_part, precision=highest)
    return (cos_real - direction * sin_imag, cos_imag + direction * sin_real)


def rotate(real_part, imag_part, cosine, sines, direction):
    return (
        real_part * cosine - direction * imag_part * sines,
        imag_part * cosine + direction * real_part * sines,
    )


def spectrum_product(left, right):
    prod_real = left[0] * right[0] - left[1] * right[1]
    prod_imag = left[0] * right[1] + left[1] * right[0]
    return (prod_real, prod_imag)


def real_inverse(real_part, imag_part, cosine, sines, pattern, length):
    return (
        jnp.einsum(pattern, cosine, real_part, precision=highest)
        - jnp.einsum(pattern, sines, imag_part, precision=highest)
    ) / length


def tables(length):
    full_rows = 2 * length // COLS
    half_rows = full_rows // 2
    period = 2 * length
    first = phase_table(full_rows, half_rows, full_rows)
    twist_cos, twist_sin = phase_table(full_rows, COLS, period)
    twist = (twist_cos[:, :, None], twist_sin[:, :, None])
    second = phase_table(COLS, COLS, COLS)
    last = phase_table(half_rows, full_rows, full_rows)
    return first, twist, second, last


def forward_spectrum(whole_seq, first, twist, second):
    length, narrow = whole_seq.shape
    half_rows = 2 * length // COLS // 2
    laid_out = whole_seq.reshape(half_rows, COLS, narrow)
    real_part, imag_part = real_transform(laid_out, first[0], first[1], "kn,nmc->kmc")
    real_part, imag_part = rotate(real_part, imag_part, twist[0], twist[1], -1.0)
    return complex_transform(
        real_part, imag_part, second[0], second[1], -1.0, "kn,anc->akc"
    )


def inverse_spectrum(real_part, imag_part, twist, second, last, length, narrow):
    real_part, imag_part = complex_transform(
        real_part, imag_part, second[0], second[1], 1.0, "kn,anc->akc"
    )
    real_part, imag_part = rotate(real_part, imag_part, twist[0], twist[1], 1.0)
    values = real_inverse(real_part, imag_part, last[0], last[1], "nk,kmc->nmc", 2 * length)
    return values.reshape(length, narrow)


def to_whole_seq(shard):
    return lax.all_to_all(shard, "seq", split_axis=1, concat_axis=0, tiled=True)


def layer(tokens, in_weight, short_taps, filter_taps, skip_gain, out_weight):
    tok_count = tokens.shape[0]
    chan_count = in_weight.shape[2]
    token_blocks = lax.all_gather(tokens, "chan", axis=0, tiled=False)
    out_block = lax.all_to_all(out_weight, "chan", split_axis=1, concat_axis=0, tiled=True)
    whole_filter = to_whole_seq(filter_taps)
    length, narrow = whole_filter.shape
    first, twist, second, last = tables(length)
    filter_tables = lax.optimization_barrier((first, twist, second))
    filter_spec = forward_spectrum(whole_filter, *filter_tables)
    flat_weight = in_weight.reshape(in_weight.shape[0], 3 * chan_count)
    token_blocks, out_block = lax.optimization_barrier((token_blocks, out_block))
    block_count, _, block_width = token_blocks.shape
    projected = jnp.einsum(
        "jtc,jcn->tn",
        token_blocks,
        flat_weight.reshape(block_count, block_width, -1),
        preferred_element_type=jnp.float32,
    )
    projected = projected.astype(jnp.bfloat16).reshape(tok_count, 3, chan_count)
    previous = from_behind(projected[-2:], "seq", 1)
    extended = jnp.concatenate([previous, projected], axis=0).astype(jnp.float32)
    short_mixed = (
        short_taps[0] * extended[2:]
        + short_taps[1] * extended[1:-1]
        + short_taps[2] * extended[:-2]
    )
    gate_out = short_mixed[:, 0]
    signal = short_mixed[:, 1] * short_mixed[:, 2]
    whole_signal = to_whole_seq(signal)
    signal_spec = forward_spectrum(whole_signal, first, twist, second)
    real_part, imag_part = spectrum_product(signal_spec, filter_spec)
    values = inverse_spectrum(real_part, imag_part, twist, second, last, length, narrow)
    convolved = lax.all_to_all(values, "seq", split_axis=0, concat_axis=1, tiled=True)
    hidden = (gate_out * (convolved + skip_gain * signal)).astype(jnp.bfloat16)
    hidden_blocks = lax.all_gather(hidden, "chan", axis=0, tiled=False)
    layer_out = jnp.einsum(
        "jtc,jcn->tn",
        hidden_blocks,
        out_block.reshape(block_count, block_width, -1),
        preferred_element_type=jnp.float32,
    )
    return layer_out.astype(jnp.bfloat16)


def solution(mesh):
    in_specs = (
        P("seq", "chan"),
        P(None, None, "chan"),
        P(None, None, "chan"),
        P("seq", "chan"),
        P("chan"),
        P("chan", None),
    )
    out_specs = P("seq", "chan")
    return jax.shard_map(layer, mesh=mesh, in_specs=in_specs, out_specs=out_specs, check_vma=False)
```

```python
import math

import jax
import jax.numpy as jnp
from jax import lax
from jax.sharding import PartitionSpec as P

COLS = 256


highest = lax.Precision.HIGH


def from_behind(shard, axis, by):
    size = lax.axis_size(axis)
    pairs = [(i, i + by) for i in range(size) if 0 <= i + by < size]
    return lax.ppermute(shard, axis, pairs)


def phase_table(row_count, col_count, period):
    row_index = jnp.arange(row_count, dtype=jnp.int32)[:, None]
    col_index = jnp.arange(col_count, dtype=jnp.int32)[None, :]
    angle = (row_index * col_index % period).astype(jnp.float32) * (2.0 * math.pi / period)
    return (jnp.cos(angle), jnp.sin(angle))


def real_transform(signal, cosine, sines, pattern):
    real_part = jnp.einsum(pattern, cosine, signal, precision=highest)
    imag_part = -jnp.einsum(pattern, sines, signal, precision=highest)
    return (real_part, imag_part)


def complex_transform(real_part, imag_part, cosine, sines, direction, pattern):
    cos_real = jnp.einsum(pattern, cosine, real_part, precision=highest)
    cos_imag = jnp.einsum(pattern, cosine, imag_part, precision=highest)
    sin_real = jnp.einsum(pattern, sines, real_part, precision=highest)
    sin_imag = jnp.einsum(pattern, sines, imag_part, precision=highest)
    return (cos_real - direction * sin_imag, cos_imag + direction * sin_real)


def rotate(real_part, imag_part, cosine, sines, direction):
    return (
        real_part * cosine - direction * imag_part * sines,
        imag_part * cosine + direction * real_part * sines,
    )


def spectrum_product(left, right):
    prod_real = left[0] * right[0] - left[1] * right[1]
    prod_imag = left[0] * right[1] + left[1] * right[0]
    return (prod_real, prod_imag)


def real_inverse(real_part, imag_part, cosine, sines, pattern, length):
    return (
        jnp.einsum(pattern, cosine, real_part, precision=highest)
        - jnp.einsum(pattern, sines, imag_part, precision=highest)
    ) / length


def tables(length):
    full_rows = 2 * length // COLS
    half_rows = full_rows // 2
    period = 2 * length
    first = phase_table(full_rows, half_rows, full_rows)
    twist_cos, twist_sin = phase_table(full_rows, COLS, period)
    twist = (twist_cos[:, :, None], twist_sin[:, :, None])
    second = phase_table(COLS, COLS, COLS)
    last = phase_table(half_rows, full_rows, full_rows)
    return first, twist, second, last


def forward_spectrum(whole_seq, first, twist, second):
    length, narrow = whole_seq.shape
    half_rows = 2 * length // COLS // 2
    laid_out = whole_seq.reshape(half_rows, COLS, narrow)
    real_part, imag_part = real_transform(laid_out, first[0], first[1], "kn,nmc->kmc")
    real_part, imag_part = rotate(real_part, imag_part, twist[0], twist[1], -1.0)
    return complex_transform(
        real_part, imag_part, second[0], second[1], -1.0, "kn,anc->akc"
    )


def inverse_spectrum(real_part, imag_part, twist, second, last, length, narrow):
    real_part, imag_part = complex_transform(
        real_part, imag_part, second[0], second[1], 1.0, "kn,anc->akc"
    )
    real_part, imag_part = rotate(real_part, imag_part, twist[0], twist[1], 1.0)
    values = real_inverse(real_part, imag_part, last[0], last[1], "nk,kmc->nmc", 2 * length)
    return values.reshape(length, narrow)


def to_whole_seq(shard):
    return lax.all_to_all(shard, "seq", split_axis=1, concat_axis=0, tiled=True)


def layer(tokens, in_weight, short_taps, filter_taps, skip_gain, out_weight):
    tok_count = tokens.shape[0]
    chan_count = in_weight.shape[2]
    token_blocks = lax.all_gather(tokens, "chan", axis=0, tiled=False)
    out_block = lax.all_to_all(out_weight, "chan", split_axis=1, concat_axis=0, tiled=True)
    whole_filter = to_whole_seq(filter_taps)
    length, narrow = whole_filter.shape
    first, twist, second, last = tables(length)
    filter_tables = lax.optimization_barrier((first, twist, second))
    filter_spec = forward_spectrum(whole_filter, *filter_tables)
    flat_weight = in_weight.reshape(in_weight.shape[0], 3 * chan_count)
    token_blocks, out_block = lax.optimization_barrier((token_blocks, out_block))
    block_count, _, block_width = token_blocks.shape
    projected = jnp.einsum(
        "jtc,jcn->tn",
        token_blocks,
        flat_weight.reshape(block_count, block_width, -1),
        preferred_element_type=jnp.float32,
    )
    projected = projected.astype(jnp.bfloat16).reshape(tok_count, 3, chan_count)
    previous = from_behind(projected[-2:], "seq", 1)
    extended = jnp.concatenate([previous, projected], axis=0).astype(jnp.float32)
    short_mixed = (
        short_taps[0] * extended[2:]
        + short_taps[1] * extended[1:-1]
        + short_taps[2] * extended[:-2]
    )
    gate_out = short_mixed[:, 0]
    signal = short_mixed[:, 1] * short_mixed[:, 2]
    whole_signal = to_whole_seq(signal.astype(jnp.bfloat16)).astype(jnp.float32)
    signal_spec = forward_spectrum(whole_signal, first, twist, second)
    real_part, imag_part = spectrum_product(signal_spec, filter_spec)
    values = inverse_spectrum(real_part, imag_part, twist, second, last, length, narrow)
    convolved = lax.all_to_all(
        values.astype(jnp.bfloat16), "seq", split_axis=0, concat_axis=1, tiled=True
    ).astype(jnp.float32)
    hidden = (gate_out * (convolved + skip_gain * signal)).astype(jnp.bfloat16)
    hidden_blocks = lax.all_gather(hidden, "chan", axis=0, tiled=False)
    layer_out = jnp.einsum(
        "jtc,jcn->tn",
        hidden_blocks,
        out_block.reshape(block_count, block_width, -1),
        preferred_element_type=jnp.float32,
    )
    return layer_out.astype(jnp.bfloat16)


def solution(mesh):
    in_specs = (
        P("seq", "chan"),
        P(None, None, "chan"),
        P(None, None, "chan"),
        P("seq", "chan"),
        P("chan"),
        P("chan", None),
    )
    out_specs = P("seq", "chan")
    return jax.shard_map(layer, mesh=mesh, in_specs=in_specs, out_specs=out_specs, check_vma=False)
```

```python
import math

import jax
import jax.numpy as jnp
from jax import lax
from jax.sharding import PartitionSpec as P

COLS = 256


highest = lax.Precision.HIGH


def from_behind(shard, axis, by):
    size = lax.axis_size(axis)
    pairs = [(i, i + by) for i in range(size) if 0 <= i + by < size]
    return lax.ppermute(shard, axis, pairs)


def phase_table(row_count, col_count, period):
    row_index = jnp.arange(row_count, dtype=jnp.int32)[:, None]
    col_index = jnp.arange(col_count, dtype=jnp.int32)[None, :]
    angle = (row_index * col_index % period).astype(jnp.float32) * (2.0 * math.pi / period)
    return (jnp.cos(angle), jnp.sin(angle))


def real_transform(signal, cosine, sines, pattern):
    real_part = jnp.einsum(pattern, cosine, signal, precision=highest)
    imag_part = -jnp.einsum(pattern, sines, signal, precision=highest)
    return (real_part, imag_part)


def complex_transform(real_part, imag_part, cosine, sines, direction, pattern):
    cos_real = jnp.einsum(pattern, cosine, real_part, precision=highest)
    cos_imag = jnp.einsum(pattern, cosine, imag_part, precision=highest)
    sin_real = jnp.einsum(pattern, sines, real_part, precision=highest)
    sin_imag = jnp.einsum(pattern, sines, imag_part, precision=highest)
    return (cos_real - direction * sin_imag, cos_imag + direction * sin_real)


def rotate(real_part, imag_part, cosine, sines, direction):
    return (
        real_part * cosine - direction * imag_part * sines,
        imag_part * cosine + direction * real_part * sines,
    )


def spectrum_product(left, right):
    prod_real = left[0] * right[0] - left[1] * right[1]
    prod_imag = left[0] * right[1] + left[1] * right[0]
    return (prod_real, prod_imag)


def real_inverse(real_part, imag_part, cosine, sines, pattern, length):
    return (
        jnp.einsum(pattern, cosine, real_part, precision=highest)
        - jnp.einsum(pattern, sines, imag_part, precision=highest)
    ) / length


def tables(length):
    full_rows = 2 * length // COLS
    half_rows = full_rows // 2
    period = 2 * length
    first = phase_table(full_rows, half_rows, full_rows)
    twist_cos, twist_sin = phase_table(full_rows, COLS, period)
    twist = (twist_cos[:, :, None], twist_sin[:, :, None])
    second = phase_table(COLS, COLS, COLS)
    last = phase_table(half_rows, full_rows, full_rows)
    return first, twist, second, last


def forward_spectrum(whole_seq, first, twist, second):
    length, narrow = whole_seq.shape
    half_rows = 2 * length // COLS // 2
    laid_out = whole_seq.reshape(half_rows, COLS, narrow)
    real_part, imag_part = real_transform(laid_out, first[0], first[1], "kn,nmc->kmc")
    real_part, imag_part = rotate(real_part, imag_part, twist[0], twist[1], -1.0)
    return complex_transform(
        real_part, imag_part, second[0], second[1], -1.0, "kn,anc->akc"
    )


def inverse_spectrum(real_part, imag_part, twist, second, last, length, narrow):
    real_part, imag_part = complex_transform(
        real_part, imag_part, second[0], second[1], 1.0, "kn,anc->akc"
    )
    real_part, imag_part = rotate(real_part, imag_part, twist[0], twist[1], 1.0)
    values = real_inverse(real_part, imag_part, last[0], last[1], "nk,kmc->nmc", 2 * length)
    return values.reshape(length, narrow)


def to_whole_seq(shard):
    return lax.all_to_all(shard, "seq", split_axis=1, concat_axis=0, tiled=True)


def layer(tokens, in_weight, short_taps, filter_taps, skip_gain, out_weight):
    tok_count = tokens.shape[0]
    chan_count = in_weight.shape[2]
    token_blocks = lax.all_gather(tokens, "chan", axis=0, tiled=False)
    seq_count = lax.axis_size("seq")
    part = out_weight.shape[0] // seq_count
    own_rows = lax.dynamic_slice_in_dim(
        out_weight, lax.axis_index("seq") * part, part, axis=0
    )
    out_rows = lax.all_to_all(own_rows, "chan", split_axis=1, concat_axis=0, tiled=True)
    whole_filter = to_whole_seq(filter_taps)
    length, narrow = whole_filter.shape
    first, twist, second, last = tables(length)
    filter_tables = lax.optimization_barrier((first, twist, second))
    filter_spec = forward_spectrum(whole_filter, *filter_tables)
    flat_weight = in_weight.reshape(in_weight.shape[0], 3 * chan_count)
    token_blocks, out_rows = lax.optimization_barrier((token_blocks, out_rows))
    block_count, _, block_width = token_blocks.shape
    projected = jnp.einsum(
        "jtc,jcn->tn",
        token_blocks,
        flat_weight.reshape(block_count, block_width, -1),
        preferred_element_type=jnp.float32,
    )
    projected = projected.astype(jnp.bfloat16).reshape(tok_count, 3, chan_count)
    previous = from_behind(projected[-2:], "seq", 1)
    extended = jnp.concatenate([previous, projected], axis=0).astype(jnp.float32)
    short_mixed = (
        short_taps[0] * extended[2:]
        + short_taps[1] * extended[1:-1]
        + short_taps[2] * extended[:-2]
    )
    gate_out = short_mixed[:, 0]
    signal = short_mixed[:, 1] * short_mixed[:, 2]
    whole_signal = to_whole_seq(signal.astype(jnp.bfloat16)).astype(jnp.float32)
    signal_spec = forward_spectrum(whole_signal, first, twist, second)
    real_part, imag_part = spectrum_product(signal_spec, filter_spec)
    values = inverse_spectrum(real_part, imag_part, twist, second, last, length, narrow)
    out_parts = lax.all_gather(out_rows, "seq", axis=0, tiled=False)
    values, out_parts = lax.optimization_barrier((values, out_parts))
    convolved = lax.all_to_all(
        values.astype(jnp.bfloat16), "seq", split_axis=0, concat_axis=1, tiled=True
    ).astype(jnp.float32)
    out_block = out_parts.reshape(seq_count, block_count, part, -1).transpose(1, 0, 2, 3)
    hidden = (gate_out * (convolved + skip_gain * signal)).astype(jnp.bfloat16)
    hidden_blocks = lax.all_gather(hidden, "chan", axis=0, tiled=False)
    layer_out = jnp.einsum(
        "jtc,jcn->tn",
        hidden_blocks,
        out_block.reshape(block_count, block_width, -1),
        preferred_element_type=jnp.float32,
    )
    return layer_out.astype(jnp.bfloat16)


def solution(mesh):
    in_specs = (
        P("seq", "chan"),
        P(None, None, "chan"),
        P(None, None, "chan"),
        P("seq", "chan"),
        P("chan"),
        P("chan", None),
    )
    out_specs = P("seq", "chan")
    return jax.shard_map(layer, mesh=mesh, in_specs=in_specs, out_specs=out_specs, check_vma=False)
```

```python
import math

import jax
import jax.numpy as jnp
from jax import lax
from jax.sharding import PartitionSpec as P

COLS = 256


highest = lax.Precision.HIGH


def from_behind(shard, axis, by):
    size = lax.axis_size(axis)
    pairs = [(i, i + by) for i in range(size) if 0 <= i + by < size]
    return lax.ppermute(shard, axis, pairs)


def phase_table(row_count, col_count, period):
    row_index = jnp.arange(row_count, dtype=jnp.int32)[:, None]
    col_index = jnp.arange(col_count, dtype=jnp.int32)[None, :]
    angle = (row_index * col_index % period).astype(jnp.float32) * (2.0 * math.pi / period)
    return (jnp.cos(angle), jnp.sin(angle))


def real_transform(signal, cosine, sines, pattern):
    real_part = jnp.einsum(pattern, cosine, signal, precision=highest)
    imag_part = -jnp.einsum(pattern, sines, signal, precision=highest)
    return (real_part, imag_part)


def complex_transform(real_part, imag_part, cosine, sines, direction, pattern):
    cos_real = jnp.einsum(pattern, cosine, real_part, precision=highest)
    cos_imag = jnp.einsum(pattern, cosine, imag_part, precision=highest)
    sin_real = jnp.einsum(pattern, sines, real_part, precision=highest)
    sin_imag = jnp.einsum(pattern, sines, imag_part, precision=highest)
    return (cos_real - direction * sin_imag, cos_imag + direction * sin_real)


def rotate(real_part, imag_part, cosine, sines, direction):
    return (
        real_part * cosine - direction * imag_part * sines,
        imag_part * cosine + direction * real_part * sines,
    )


def spectrum_product(left, right):
    prod_real = left[0] * right[0] - left[1] * right[1]
    prod_imag = left[0] * right[1] + left[1] * right[0]
    return (prod_real, prod_imag)


def real_inverse(real_part, imag_part, cosine, sines, pattern, length):
    return (
        jnp.einsum(pattern, cosine, real_part, precision=highest)
        - jnp.einsum(pattern, sines, imag_part, precision=highest)
    ) / length


def tables(length):
    full_rows = 2 * length // COLS
    half_rows = full_rows // 2
    period = 2 * length
    first = phase_table(full_rows, half_rows, full_rows)
    twist_cos, twist_sin = phase_table(full_rows, COLS, period)
    twist = (twist_cos[:, :, None], twist_sin[:, :, None])
    second = phase_table(COLS, COLS, COLS)
    last = phase_table(half_rows, full_rows, full_rows)
    return first, twist, second, last


def forward_spectrum(whole_seq, first, twist, second):
    length, narrow = whole_seq.shape
    half_rows = 2 * length // COLS // 2
    laid_out = whole_seq.reshape(half_rows, COLS, narrow)
    real_part, imag_part = real_transform(laid_out, first[0], first[1], "kn,nmc->kmc")
    real_part, imag_part = rotate(real_part, imag_part, twist[0], twist[1], -1.0)
    return complex_transform(
        real_part, imag_part, second[0], second[1], -1.0, "kn,anc->akc"
    )


def inverse_spectrum(real_part, imag_part, twist, second, last, length, narrow):
    real_part, imag_part = complex_transform(
        real_part, imag_part, second[0], second[1], 1.0, "kn,anc->akc"
    )
    real_part, imag_part = rotate(real_part, imag_part, twist[0], twist[1], 1.0)
    values = real_inverse(real_part, imag_part, last[0], last[1], "nk,kmc->nmc", 2 * length)
    return values.reshape(length, narrow)


def to_whole_seq(shard):
    return lax.all_to_all(shard, "seq", split_axis=1, concat_axis=0, tiled=True)


def layer(tokens, in_weight, short_taps, filter_taps, skip_gain, out_weight):
    tok_count = tokens.shape[0]
    chan_count = in_weight.shape[2]
    token_blocks = lax.all_gather(tokens, "chan", axis=0, tiled=False)
    seq_count = lax.axis_size("seq")
    part = out_weight.shape[0] // seq_count
    own_rows = lax.dynamic_slice_in_dim(
        out_weight, lax.axis_index("seq") * part, part, axis=0
    )
    out_rows = lax.all_to_all(own_rows, "chan", split_axis=1, concat_axis=0, tiled=True)
    whole_filter = to_whole_seq(filter_taps)
    length, narrow = whole_filter.shape
    first, twist, second, last = tables(length)
    filter_tables = lax.optimization_barrier((first, twist, second))
    filter_spec = forward_spectrum(whole_filter, *filter_tables)
    flat_weight = in_weight.reshape(in_weight.shape[0], 3 * chan_count)
    token_blocks, out_rows = lax.optimization_barrier((token_blocks, out_rows))
    block_count, _, block_width = token_blocks.shape
    projected = jnp.einsum(
        "jtc,jcn->tn",
        token_blocks,
        flat_weight.reshape(block_count, block_width, -1),
        preferred_element_type=jnp.float32,
    )
    projected = projected.astype(jnp.bfloat16).reshape(tok_count, 3, chan_count)
    previous = from_behind(projected[-2:], "seq", 1)
    extended = jnp.concatenate([previous, projected], axis=0).astype(jnp.float32)
    short_mixed = (
        short_taps[0] * extended[2:]
        + short_taps[1] * extended[1:-1]
        + short_taps[2] * extended[:-2]
    )
    gate_out = short_mixed[:, 0]
    signal = short_mixed[:, 1] * short_mixed[:, 2]
    whole_signal = to_whole_seq(signal.astype(jnp.bfloat16)).astype(jnp.float32)
    signal_spec = forward_spectrum(whole_signal, first, twist, second)
    real_part, imag_part = spectrum_product(signal_spec, filter_spec)
    values = inverse_spectrum(real_part, imag_part, twist, second, last, length, narrow)
    seq_tiled = jnp.broadcast_to(out_rows[None], (seq_count,) + out_rows.shape)
    values, seq_tiled = lax.optimization_barrier((values, seq_tiled))
    out_parts = lax.all_to_all(seq_tiled, "seq", split_axis=0, concat_axis=0, tiled=True)
    convolved = lax.all_to_all(
        values.astype(jnp.bfloat16), "seq", split_axis=0, concat_axis=1, tiled=True
    ).astype(jnp.float32)
    out_block = out_parts.reshape(seq_count, block_count, part, -1).transpose(1, 0, 2, 3)
    hidden = (gate_out * (convolved + skip_gain * signal)).astype(jnp.bfloat16)
    hidden_blocks = lax.all_gather(hidden, "chan", axis=0, tiled=False)
    layer_out = jnp.einsum(
        "jtc,jcn->tn",
        hidden_blocks,
        out_block.reshape(block_count, block_width, -1),
        preferred_element_type=jnp.float32,
    )
    return layer_out.astype(jnp.bfloat16)


def solution(mesh):
    in_specs = (
        P("seq", "chan"),
        P(None, None, "chan"),
        P(None, None, "chan"),
        P("seq", "chan"),
        P("chan"),
        P("chan", None),
    )
    out_specs = P("seq", "chan")
    return jax.shard_map(layer, mesh=mesh, in_specs=in_specs, out_specs=out_specs, check_vma=False)
```

```python
import math

import jax
import jax.numpy as jnp
from jax import lax
from jax.sharding import PartitionSpec as P

COLS = 256


highest = lax.Precision.HIGH


def from_behind(shard, axis, by):
    size = lax.axis_size(axis)
    pairs = [(i, i + by) for i in range(size) if 0 <= i + by < size]
    return lax.ppermute(shard, axis, pairs)


def phase_table(row_count, col_count, period):
    row_index = jnp.arange(row_count, dtype=jnp.int32)[:, None]
    col_index = jnp.arange(col_count, dtype=jnp.int32)[None, :]
    angle = (row_index * col_index % period).astype(jnp.float32) * (2.0 * math.pi / period)
    return (jnp.cos(angle), jnp.sin(angle))


def real_transform(signal, cosine, sines, pattern):
    real_part = jnp.einsum(pattern, cosine, signal, precision=lax.Precision.DEFAULT)
    imag_part = -jnp.einsum(pattern, sines, signal, precision=lax.Precision.DEFAULT)
    return (real_part, imag_part)


def complex_transform(real_part, imag_part, cosine, sines, direction, pattern):
    cos_real = jnp.einsum(pattern, cosine, real_part, precision=highest)
    cos_imag = jnp.einsum(pattern, cosine, imag_part, precision=highest)
    sin_real = jnp.einsum(pattern, sines, real_part, precision=highest)
    sin_imag = jnp.einsum(pattern, sines, imag_part, precision=highest)
    return (cos_real - direction * sin_imag, cos_imag + direction * sin_real)


def rotate(real_part, imag_part, cosine, sines, direction):
    return (
        real_part * cosine - direction * imag_part * sines,
        imag_part * cosine + direction * real_part * sines,
    )


def spectrum_product(left, right):
    prod_real = left[0] * right[0] - left[1] * right[1]
    prod_imag = left[0] * right[1] + left[1] * right[0]
    return (prod_real, prod_imag)


def real_inverse(real_part, imag_part, cosine, sines, pattern, length):
    return (
        jnp.einsum(pattern, cosine, real_part, precision=lax.Precision.DEFAULT)
        - jnp.einsum(pattern, sines, imag_part, precision=lax.Precision.DEFAULT)
    ) / length


def tables(length):
    full_rows = 2 * length // COLS
    half_rows = full_rows // 2
    period = 2 * length
    first = phase_table(full_rows, half_rows, full_rows)
    twist_cos, twist_sin = phase_table(full_rows, COLS, period)
    twist = (twist_cos[:, :, None], twist_sin[:, :, None])
    second = phase_table(COLS, COLS, COLS)
    last = phase_table(half_rows, full_rows, full_rows)
    return first, twist, second, last


def forward_spectrum(whole_seq, first, twist, second):
    length, narrow = whole_seq.shape
    half_rows = 2 * length // COLS // 2
    laid_out = whole_seq.reshape(half_rows, COLS, narrow)
    real_part, imag_part = real_transform(laid_out, first[0], first[1], "kn,nmc->kmc")
    real_part, imag_part = rotate(real_part, imag_part, twist[0], twist[1], -1.0)
    return complex_transform(
        real_part, imag_part, second[0], second[1], -1.0, "kn,anc->akc"
    )


def inverse_spectrum(real_part, imag_part, twist, second, last, length, narrow):
    real_part, imag_part = complex_transform(
        real_part, imag_part, second[0], second[1], 1.0, "kn,anc->akc"
    )
    real_part, imag_part = rotate(real_part, imag_part, twist[0], twist[1], 1.0)
    values = real_inverse(real_part, imag_part, last[0], last[1], "nk,kmc->nmc", 2 * length)
    return values.reshape(length, narrow)


def to_whole_seq(shard):
    return lax.all_to_all(shard, "seq", split_axis=1, concat_axis=0, tiled=True)


def layer(tokens, in_weight, short_taps, filter_taps, skip_gain, out_weight):
    tok_count = tokens.shape[0]
    chan_count = in_weight.shape[2]
    token_blocks = lax.all_gather(tokens, "chan", axis=0, tiled=False)
    seq_count = lax.axis_size("seq")
    part = out_weight.shape[0] // seq_count
    own_rows = lax.dynamic_slice_in_dim(
        out_weight, lax.axis_index("seq") * part, part, axis=0
    )
    out_rows = lax.all_to_all(own_rows, "chan", split_axis=1, concat_axis=0, tiled=True)
    whole_filter = to_whole_seq(filter_taps)
    length, narrow = whole_filter.shape
    first, twist, second, last = tables(length)
    filter_tables = lax.optimization_barrier((first, twist, second))
    filter_spec = forward_spectrum(whole_filter, *filter_tables)
    flat_weight = in_weight.reshape(in_weight.shape[0], 3 * chan_count)
    token_blocks, out_rows = lax.optimization_barrier((token_blocks, out_rows))
    block_count, _, block_width = token_blocks.shape
    projected = jnp.einsum(
        "jtc,jcn->tn",
        token_blocks,
        flat_weight.reshape(block_count, block_width, -1),
        preferred_element_type=jnp.float32,
    )
    projected = projected.astype(jnp.bfloat16).reshape(tok_count, 3, chan_count)
    previous = from_behind(projected[-2:], "seq", 1)
    extended = jnp.concatenate([previous, projected], axis=0).astype(jnp.float32)
    short_mixed = (
        short_taps[0] * extended[2:]
        + short_taps[1] * extended[1:-1]
        + short_taps[2] * extended[:-2]
    )
    gate_out = short_mixed[:, 0]
    signal = short_mixed[:, 1] * short_mixed[:, 2]
    whole_signal = to_whole_seq(signal.astype(jnp.bfloat16)).astype(jnp.float32)
    signal_spec = forward_spectrum(whole_signal, first, twist, second)
    real_part, imag_part = spectrum_product(signal_spec, filter_spec)
    values = inverse_spectrum(real_part, imag_part, twist, second, last, length, narrow)
    seq_tiled = jnp.broadcast_to(out_rows[None], (seq_count,) + out_rows.shape)
    values, seq_tiled = lax.optimization_barrier((values, seq_tiled))
    out_parts = lax.all_to_all(seq_tiled, "seq", split_axis=0, concat_axis=0, tiled=True)
    convolved = lax.all_to_all(
        values.astype(jnp.bfloat16), "seq", split_axis=0, concat_axis=1, tiled=True
    ).astype(jnp.float32)
    out_block = out_parts.reshape(seq_count, block_count, part, -1).transpose(1, 0, 2, 3)
    hidden = (gate_out * (convolved + skip_gain * signal)).astype(jnp.bfloat16)
    hidden_blocks = lax.all_gather(hidden, "chan", axis=0, tiled=False)
    layer_out = jnp.einsum(
        "jtc,jcn->tn",
        hidden_blocks,
        out_block.reshape(block_count, block_width, -1),
        preferred_element_type=jnp.float32,
    )
    return layer_out.astype(jnp.bfloat16)


def solution(mesh):
    in_specs = (
        P("seq", "chan"),
        P(None, None, "chan"),
        P(None, None, "chan"),
        P("seq", "chan"),
        P("chan"),
        P("chan", None),
    )
    out_specs = P("seq", "chan")
    return jax.shard_map(layer, mesh=mesh, in_specs=in_specs, out_specs=out_specs, check_vma=False)
```

```python
import math

import jax
import jax.numpy as jnp
from jax import lax
from jax.sharding import PartitionSpec as P

COLS = 256


highest = lax.Precision.HIGH


def from_behind(shard, axis, by):
    size = lax.axis_size(axis)
    pairs = [(i, i + by) for i in range(size) if 0 <= i + by < size]
    return lax.ppermute(shard, axis, pairs)


def phase_table(row_count, col_count, period):
    row_index = jnp.arange(row_count, dtype=jnp.int32)[:, None]
    col_index = jnp.arange(col_count, dtype=jnp.int32)[None, :]
    angle = (row_index * col_index % period).astype(jnp.float32) * (2.0 * math.pi / period)
    return (jnp.cos(angle), jnp.sin(angle))


def real_transform(signal, cosine, sines, pattern):
    real_part = jnp.einsum(pattern, cosine, signal, precision=lax.Precision.DEFAULT)
    imag_part = -jnp.einsum(pattern, sines, signal, precision=lax.Precision.DEFAULT)
    return (real_part, imag_part)


def complex_transform(real_part, imag_part, cosine, sines, direction, pattern, precision=highest):
    cos_real = jnp.einsum(pattern, cosine, real_part, precision=precision)
    cos_imag = jnp.einsum(pattern, cosine, imag_part, precision=precision)
    sin_real = jnp.einsum(pattern, sines, real_part, precision=precision)
    sin_imag = jnp.einsum(pattern, sines, imag_part, precision=precision)
    return (cos_real - direction * sin_imag, cos_imag + direction * sin_real)


def rotate(real_part, imag_part, cosine, sines, direction):
    return (
        real_part * cosine - direction * imag_part * sines,
        imag_part * cosine + direction * real_part * sines,
    )


def spectrum_product(left, right):
    prod_real = left[0] * right[0] - left[1] * right[1]
    prod_imag = left[0] * right[1] + left[1] * right[0]
    return (prod_real, prod_imag)


def real_inverse(real_part, imag_part, cosine, sines, pattern, length):
    return (
        jnp.einsum(pattern, cosine, real_part, precision=lax.Precision.DEFAULT)
        - jnp.einsum(pattern, sines, imag_part, precision=lax.Precision.DEFAULT)
    ) / length


def tables(length):
    full_rows = 2 * length // COLS
    half_rows = full_rows // 2
    period = 2 * length
    first = phase_table(full_rows, half_rows, full_rows)
    twist_cos, twist_sin = phase_table(full_rows, COLS, period)
    twist = (twist_cos[:, :, None], twist_sin[:, :, None])
    second = phase_table(COLS, COLS, COLS)
    last = phase_table(half_rows, full_rows, full_rows)
    return first, twist, second, last


def forward_spectrum(whole_seq, first, twist, second, precision=highest):
    length, narrow = whole_seq.shape
    half_rows = 2 * length // COLS // 2
    laid_out = whole_seq.reshape(half_rows, COLS, narrow)
    real_part, imag_part = real_transform(laid_out, first[0], first[1], "kn,nmc->kmc")
    real_part, imag_part = rotate(real_part, imag_part, twist[0], twist[1], -1.0)
    return complex_transform(
        real_part, imag_part, second[0], second[1], -1.0, "kn,anc->akc", precision
    )


def inverse_spectrum(real_part, imag_part, twist, second, last, length, narrow):
    real_part, imag_part = complex_transform(
        real_part, imag_part, second[0], second[1], 1.0, "kn,anc->akc"
    )
    real_part, imag_part = rotate(real_part, imag_part, twist[0], twist[1], 1.0)
    values = real_inverse(real_part, imag_part, last[0], last[1], "nk,kmc->nmc", 2 * length)
    return values.reshape(length, narrow)


def to_whole_seq(shard):
    return lax.all_to_all(shard, "seq", split_axis=1, concat_axis=0, tiled=True)


def layer(tokens, in_weight, short_taps, filter_taps, skip_gain, out_weight):
    tok_count = tokens.shape[0]
    chan_count = in_weight.shape[2]
    token_blocks = lax.all_gather(tokens, "chan", axis=0, tiled=False)
    seq_count = lax.axis_size("seq")
    part = out_weight.shape[0] // seq_count
    own_rows = lax.dynamic_slice_in_dim(
        out_weight, lax.axis_index("seq") * part, part, axis=0
    )
    out_rows = lax.all_to_all(own_rows, "chan", split_axis=1, concat_axis=0, tiled=True)
    whole_filter = to_whole_seq(filter_taps)
    length, narrow = whole_filter.shape
    first, twist, second, last = tables(length)
    filter_tables = lax.optimization_barrier((first, twist, second))
    filter_spec = forward_spectrum(whole_filter, *filter_tables, precision=lax.Precision.DEFAULT)
    flat_weight = in_weight.reshape(in_weight.shape[0], 3 * chan_count)
    token_blocks, out_rows = lax.optimization_barrier((token_blocks, out_rows))
    block_count, _, block_width = token_blocks.shape
    projected = jnp.einsum(
        "jtc,jcn->tn",
        token_blocks,
        flat_weight.reshape(block_count, block_width, -1),
        preferred_element_type=jnp.float32,
    )
    projected = projected.astype(jnp.bfloat16).reshape(tok_count, 3, chan_count)
    previous = from_behind(projected[-2:], "seq", 1)
    extended = jnp.concatenate([previous, projected], axis=0).astype(jnp.float32)
    short_mixed = (
        short_taps[0] * extended[2:]
        + short_taps[1] * extended[1:-1]
        + short_taps[2] * extended[:-2]
    )
    gate_out = short_mixed[:, 0]
    signal = short_mixed[:, 1] * short_mixed[:, 2]
    whole_signal = to_whole_seq(signal.astype(jnp.bfloat16)).astype(jnp.float32)
    signal_spec = forward_spectrum(whole_signal, first, twist, second)
    real_part, imag_part = spectrum_product(signal_spec, filter_spec)
    values = inverse_spectrum(real_part, imag_part, twist, second, last, length, narrow)
    seq_tiled = jnp.broadcast_to(out_rows[None], (seq_count,) + out_rows.shape)
    values, seq_tiled = lax.optimization_barrier((values, seq_tiled))
    out_parts = lax.all_to_all(seq_tiled, "seq", split_axis=0, concat_axis=0, tiled=True)
    convolved = lax.all_to_all(
        values.astype(jnp.bfloat16), "seq", split_axis=0, concat_axis=1, tiled=True
    ).astype(jnp.float32)
    out_block = out_parts.reshape(seq_count, block_count, part, -1).transpose(1, 0, 2, 3)
    hidden = (gate_out * (convolved + skip_gain * signal)).astype(jnp.bfloat16)
    hidden_blocks = lax.all_gather(hidden, "chan", axis=0, tiled=False)
    layer_out = jnp.einsum(
        "jtc,jcn->tn",
        hidden_blocks,
        out_block.reshape(block_count, block_width, -1),
        preferred_element_type=jnp.float32,
    )
    return layer_out.astype(jnp.bfloat16)


def solution(mesh):
    in_specs = (
        P("seq", "chan"),
        P(None, None, "chan"),
        P(None, None, "chan"),
        P("seq", "chan"),
        P("chan"),
        P("chan", None),
    )
    out_specs = P("seq", "chan")
    return jax.shard_map(layer, mesh=mesh, in_specs=in_specs, out_specs=out_specs, check_vma=False)
```

```python
import math

import jax
import jax.numpy as jnp
from jax import lax
from jax.sharding import PartitionSpec as P

COLS = 256


highest = lax.Precision.HIGH


def from_behind(shard, axis, by):
    size = lax.axis_size(axis)
    pairs = [(i, i + by) for i in range(size) if 0 <= i + by < size]
    return lax.ppermute(shard, axis, pairs)


def phase_table(row_count, col_count, period):
    row_index = jnp.arange(row_count, dtype=jnp.int32)[:, None]
    col_index = jnp.arange(col_count, dtype=jnp.int32)[None, :]
    angle = (row_index * col_index % period).astype(jnp.float32) * (2.0 * math.pi / period)
    return (jnp.cos(angle), jnp.sin(angle))


def real_transform(signal, cosine, sines, pattern):
    real_part = jnp.einsum(pattern, cosine, signal, precision=lax.Precision.DEFAULT)
    imag_part = -jnp.einsum(pattern, sines, signal, precision=lax.Precision.DEFAULT)
    return (real_part, imag_part)


def complex_transform(real_part, imag_part, cosine, sines, direction, pattern, precision=highest):
    cos_real = jnp.einsum(pattern, cosine, real_part, precision=precision)
    cos_imag = jnp.einsum(pattern, cosine, imag_part, precision=precision)
    sin_real = jnp.einsum(pattern, sines, real_part, precision=precision)
    sin_imag = jnp.einsum(pattern, sines, imag_part, precision=precision)
    return (cos_real - direction * sin_imag, cos_imag + direction * sin_real)


def rotate(real_part, imag_part, cosine, sines, direction):
    return (
        real_part * cosine - direction * imag_part * sines,
        imag_part * cosine + direction * real_part * sines,
    )


def spectrum_product(left, right):
    prod_real = left[0] * right[0] - left[1] * right[1]
    prod_imag = left[0] * right[1] + left[1] * right[0]
    return (prod_real, prod_imag)


def real_inverse(real_part, imag_part, cosine, sines, pattern, length):
    return (
        jnp.einsum(pattern, cosine, real_part, precision=lax.Precision.DEFAULT)
        - jnp.einsum(pattern, sines, imag_part, precision=lax.Precision.DEFAULT)
    ) / length


def tables(length):
    full_rows = 2 * length // COLS
    half_rows = full_rows // 2
    period = 2 * length
    first = phase_table(full_rows, half_rows, full_rows)
    twist_cos, twist_sin = phase_table(full_rows, COLS, period)
    twist = (twist_cos[:, :, None], twist_sin[:, :, None])
    second = phase_table(COLS, COLS, COLS)
    last = phase_table(half_rows, full_rows, full_rows)
    return first, twist, second, last


def forward_spectrum(whole_seq, first, twist, second, precision=highest):
    length, narrow = whole_seq.shape
    half_rows = 2 * length // COLS // 2
    laid_out = whole_seq.reshape(half_rows, COLS, narrow)
    real_part, imag_part = real_transform(laid_out, first[0], first[1], "kn,nmc->kmc")
    real_part, imag_part = rotate(real_part, imag_part, twist[0], twist[1], -1.0)
    return complex_transform(
        real_part, imag_part, second[0], second[1], -1.0, "kn,anc->akc", precision
    )


def inverse_spectrum(real_part, imag_part, twist, second, last, length, narrow):
    real_part, imag_part = complex_transform(
        real_part, imag_part, second[0], second[1], 1.0, "kn,anc->akc", lax.Precision.DEFAULT
    )
    real_part, imag_part = rotate(real_part, imag_part, twist[0], twist[1], 1.0)
    values = real_inverse(real_part, imag_part, last[0], last[1], "nk,kmc->nmc", 2 * length)
    return values.reshape(length, narrow)


def to_whole_seq(shard):
    return lax.all_to_all(shard, "seq", split_axis=1, concat_axis=0, tiled=True)


def layer(tokens, in_weight, short_taps, filter_taps, skip_gain, out_weight):
    tok_count = tokens.shape[0]
    chan_count = in_weight.shape[2]
    token_blocks = lax.all_gather(tokens, "chan", axis=0, tiled=False)
    seq_count = lax.axis_size("seq")
    part = out_weight.shape[0] // seq_count
    own_rows = lax.dynamic_slice_in_dim(
        out_weight, lax.axis_index("seq") * part, part, axis=0
    )
    out_rows = lax.all_to_all(own_rows, "chan", split_axis=1, concat_axis=0, tiled=True)
    whole_filter = to_whole_seq(filter_taps)
    length, narrow = whole_filter.shape
    first, twist, second, last = tables(length)
    filter_tables = lax.optimization_barrier((first, twist, second))
    filter_spec = forward_spectrum(whole_filter, *filter_tables, precision=lax.Precision.DEFAULT)
    flat_weight = in_weight.reshape(in_weight.shape[0], 3 * chan_count)
    token_blocks, out_rows = lax.optimization_barrier((token_blocks, out_rows))
    block_count, _, block_width = token_blocks.shape
    projected = jnp.einsum(
        "jtc,jcn->tn",
        token_blocks,
        flat_weight.reshape(block_count, block_width, -1),
        preferred_element_type=jnp.float32,
    )
    projected = projected.astype(jnp.bfloat16).reshape(tok_count, 3, chan_count)
    previous = from_behind(projected[-2:], "seq", 1)
    extended = jnp.concatenate([previous, projected], axis=0).astype(jnp.float32)
    short_mixed = (
        short_taps[0] * extended[2:]
        + short_taps[1] * extended[1:-1]
        + short_taps[2] * extended[:-2]
    )
    gate_out = short_mixed[:, 0]
    signal = short_mixed[:, 1] * short_mixed[:, 2]
    whole_signal = to_whole_seq(signal.astype(jnp.bfloat16)).astype(jnp.float32)
    signal_spec = forward_spectrum(
        whole_signal, first, twist, second, precision=lax.Precision.DEFAULT
    )
    real_part, imag_part = spectrum_product(signal_spec, filter_spec)
    values = inverse_spectrum(real_part, imag_part, twist, second, last, length, narrow)
    seq_tiled = jnp.broadcast_to(out_rows[None], (seq_count,) + out_rows.shape)
    values, seq_tiled = lax.optimization_barrier((values, seq_tiled))
    out_parts = lax.all_to_all(seq_tiled, "seq", split_axis=0, concat_axis=0, tiled=True)
    convolved = lax.all_to_all(
        values.astype(jnp.bfloat16), "seq", split_axis=0, concat_axis=1, tiled=True
    ).astype(jnp.float32)
    out_block = out_parts.reshape(seq_count, block_count, part, -1).transpose(1, 0, 2, 3)
    hidden = (gate_out * (convolved + skip_gain * signal)).astype(jnp.bfloat16)
    hidden_blocks = lax.all_gather(hidden, "chan", axis=0, tiled=False)
    layer_out = jnp.einsum(
        "jtc,jcn->tn",
        hidden_blocks,
        out_block.reshape(block_count, block_width, -1),
        preferred_element_type=jnp.float32,
    )
    return layer_out.astype(jnp.bfloat16)


def solution(mesh):
    in_specs = (
        P("seq", "chan"),
        P(None, None, "chan"),
        P(None, None, "chan"),
        P("seq", "chan"),
        P("chan"),
        P("chan", None),
    )
    out_specs = P("seq", "chan")
    return jax.shard_map(layer, mesh=mesh, in_specs=in_specs, out_specs=out_specs, check_vma=False)
```
